1024 devices in a mesh: seq: 32 (over y, x_hi, core), tp: 32 (over z, x_lo).
Axes of the slice: x: 4 (x_hi: 2, x_lo: 2; x = x_hi * 2 + x_lo), y: 8, z: 16, core: 2. Of those that a mesh axis runs over, the one named last changes fastest.
Arguments:
- tokens: bfloat16 [4096, 8192], P('seq', 'tp'), may hold values from -6 to 6
- w_gate: bfloat16 [8192, 8192], P(None, 'tp'), may hold values from -0.125 to 0.125
- w_conv_in: bfloat16 [8192, 8192], P(None, 'tp'), may hold values from -0.125 to 0.125
- conv_weight: float32 [4, 8192], P(None, 'tp'), may hold values from -3 to 3
- conv_bias: float32 [8192], P('tp'), may hold values from -3 to 3
- score_head: bfloat16 [10, 8192], P(None, 'tp'), may hold values from -6 to 6
- targets: int32 [4096], P('seq'), may hold values from 0 to 9
- loss_mask: int32 [4096], P('seq'), may hold values 0 or 1
Outputs:
- gated: bfloat16 [4096, 8192], P('seq', 'tp')
- d_tokens: bfloat16 [4096, 8192], P('seq', 'tp')
The draws below stay inside these ranges and needn't reach their ends.
All inputs are finite; a program needn't handle non-finite values. No bound on the sum of `loss_mask` on one device may be relied on, other than what follows from the above.
Results may differ from the reference program's by a relative error of at most 0.03.
Values may be sent and summed in bfloat16 or wider, within the bound.
No kernel may reach another device: no remote copies, remote signals or barrier semaphores. Data moves between devices by JAX's collectives and lax.ppermute only.
A program may use at most 32 MiB of HBM per device.

```python
import jax
import jax.numpy as jnp
from jax import lax

D = 8192
CX = 8192
KW = 4
SCORES = 10
LEN = 4096
N_TP = 32


def place_ends(values, rng, low, top_value):
    shape = values.shape
    spot = [jax.random.randint(jax.random.fold_in(rng, axis), (), 0, shape[axis]) for axis in range(len(shape))]
    values = values.at[tuple(spot)].set(low)
    longest = shape.index(max(shape))
    spot[longest] = (spot[longest] + 1) % shape[longest]
    return values.at[tuple(spot)].set(top_value)


def raised(result, rng, source, target, blocks, factor):
    def block_of(dim):
        return (jnp.arange(result.shape[dim]) // (result.shape[dim] // blocks)).reshape((-1,) + (1,) * (result.ndim - 1 - dim))

    one_side = jax.random.permutation(rng, blocks)[block_of(target)]
    second = (block_of(target) + blocks // 2) % blocks
    return jnp.where((block_of(source) == one_side) | (block_of(source) == second), factor * result, result)


def steps_of(key, dims, split, low, top_value):
    factor_of = 1.0
    for axis_at, blocks in split:
        heights = jax.random.uniform(jax.random.fold_in(jax.random.fold_in(key, 6), axis_at), (blocks,), jnp.float32, low / len(split), top_value / len(split))
        factor_of = factor_of * jnp.repeat(jnp.exp(heights), dims[axis_at] // blocks).reshape((-1,) + (1,) * (len(dims) - 1 - axis_at))
    return factor_of


def noise(rng, shape, scale, limit, pieces=(), held_as=jnp.bfloat16):
    result = scale * jax.random.normal(rng, shape, jnp.float32)
    if pieces:
        result = result * steps_of(rng, shape, pieces, -0.22, 0.18)
    return jnp.clip(result, -limit, limit).astype(held_as)


def noise_with(rng, shape, scale, bound, cuts, heavy, held_as=jnp.bfloat16):
    array = scale * jax.random.normal(rng, shape, jnp.float32)
    if cuts:
        array = array * steps_of(rng, shape, cuts, -0.22, 0.18)
    return jnp.clip(raised(array, jax.random.fold_in(rng, 3), *heavy), -bound, bound).astype(held_as)


def setup_inputs(seed: int = 0) -> dict:
    streams_of = jax.random.split(jax.random.key(seed), 9)
    return {
        "tokens": noise(streams_of[0], (LEN, D), 1.0, 6.0, ((0, 32), (1, 32))),
        "w_gate": noise_with(streams_of[1], (D, CX), D ** -0.5, 0.125, ((1, 32),), (1, 0, 32, 2.75)),
        "w_conv_in": noise_with(streams_of[2], (D, CX), D ** -0.5, 0.125, ((1, 32),), (1, 0, 32, 2.75)),
        "conv_weight": noise(streams_of[3], (KW, CX), 0.5, 3.0, ((1, 32),), jnp.float32),
        "conv_bias": noise(streams_of[4], (CX,), 0.5, 3.0, ((0, 32),), jnp.float32),
        "score_head": noise(streams_of[5], (SCORES, CX), 1.0, 6.0, ((1, 32),)),
        "targets": place_ends(jax.random.randint(streams_of[6], (LEN,), 0, SCORES), jax.random.fold_in(streams_of[6], 1), 0, SCORES - 1).astype(jnp.int32),
        "loss_mask": place_ends((jax.random.randint(streams_of[7], (LEN,), 0, 2) < 1).astype(jnp.int32), jax.random.fold_in(streams_of[7], 1), 0, 1),
    }


def silu_slope(value):
    sig = jax.nn.sigmoid(value)
    return sig * (1.0 + value * (1.0 - sig))


def reference(tokens, w_gate, w_conv_in, conv_weight, conv_bias, score_head, targets, loss_mask):
    gate16 = jnp.dot(tokens, w_gate, preferred_element_type=jnp.float32).astype(jnp.bfloat16)
    gate16 = lax.optimization_barrier(gate16)
    zgate = gate16.astype(jnp.float32)
    xin16 = jnp.dot(tokens, w_conv_in, preferred_element_type=jnp.float32).astype(jnp.bfloat16)
    xin16 = lax.optimization_barrier(xin16)
    padded = jnp.concatenate([jnp.zeros((KW - 1, CX), jnp.float32), xin16.astype(jnp.float32)], axis=0)
    conv_out = conv_bias[None, :] + sum(conv_weight[k][None, :] * padded[k:k + LEN] for k in range(KW))
    active = jax.nn.silu(conv_out)
    sgate = jax.nn.silu(zgate)
    gated = (active * sgate).astype(jnp.bfloat16)
    onehot = (targets[:, None] == jnp.arange(SCORES, dtype=jnp.int32)[None, :]).astype(jnp.bfloat16)
    picked = jnp.dot(onehot, score_head, preferred_element_type=jnp.float32)
    dgated = loss_mask.astype(jnp.float32)[:, None] * picked
    dgate16 = (dgated * active * silu_slope(zgate)).astype(jnp.bfloat16)
    dconv = dgated * sgate * silu_slope(conv_out)
    extended = jnp.concatenate([dconv, jnp.zeros((KW - 1, CX), jnp.float32)], axis=0)
    dxin = sum(conv_weight[k][None, :] * extended[KW - 1 - k:KW - 1 - k + LEN] for k in range(KW))
    dxin16 = dxin.astype(jnp.bfloat16)
    spec = (((1,), (1,)), ((), ()))
    block = CX // N_TP

    def add_block(index, total):
        start = (index * block).astype(jnp.int32)
        gate_part = lax.dynamic_slice_in_dim(dgate16, start, block, 1)
        xin_part = lax.dynamic_slice_in_dim(dxin16, start, block, 1)
        wg_part = lax.dynamic_slice_in_dim(w_gate, start, block, 1)
        wc_part = lax.dynamic_slice_in_dim(w_conv_in, start, block, 1)
        part = lax.dot_general(gate_part, wg_part, spec, preferred_element_type=jnp.float32)
        part = part + lax.dot_general(xin_part, wc_part, spec, preferred_element_type=jnp.float32)
        part16 = lax.optimization_barrier(part.astype(jnp.bfloat16))
        return total + part16.astype(jnp.float32)

    total = lax.fori_loop(jnp.int32(0), jnp.int32(N_TP), add_block, jnp.zeros((LEN, D), jnp.float32))
    return gated, total.astype(jnp.bfloat16)
```

```python
import jax
import jax.numpy as jnp
from jax import lax
from jax.sharding import Mesh
from jax.sharding import PartitionSpec as P

TP = ("tz", "tx")


def shifted(block, axis, distance):
    size = lax.axis_size(axis)
    return lax.ppermute(block, axis, [(i, (i + distance) % size) for i in range(size)])


def halves_in_order(mine, other):
    first = lax.axis_index("tx") == 0
    return jnp.where(first, jnp.concatenate([mine, other], 1), jnp.concatenate([other, mine], 1))


def gather_features(tokens):
    rows = tokens.shape[0]
    pair = halves_in_order(tokens, shifted(tokens, "tx", 1))
    count = lax.axis_size("tz")
    blocks = [pair] * count
    ahead = pair
    behind = pair
    for step in range(1, count // 2 + 1):
        ahead = shifted(ahead, "tz", 1)
        blocks[-step % count] = ahead
        if step < count - step:
            behind = shifted(behind, "tz", -1)
            blocks[step] = behind
    stacked = jnp.stack(blocks, 0)
    doubled = jnp.concatenate([stacked, stacked], 0)
    start = (count - lax.axis_index("tz")) % count
    ordered = lax.dynamic_slice_in_dim(doubled, start, count, 0)
    return ordered.transpose(1, 0, 2).reshape(rows, -1)


def scatter_features(terms16):
    rows = terms16.shape[0]
    count = lax.axis_size("tz")
    width = terms16.shape[1] // count
    per_dest = terms16.reshape(rows, count, width).transpose(1, 0, 2)
    doubled = jnp.concatenate([per_dest, per_dest], 0)
    own = lax.dynamic_slice_in_dim(doubled, lax.axis_index("tz"), count, 0).astype(jnp.float32)
    right = count - 1 - count // 2
    left = count // 2
    total = own[0]
    if right > 0:
        acc = own[right]
        for step in range(1, right):
            acc = shifted(acc.astype(jnp.bfloat16), "tz", 1).astype(jnp.float32) + own[right - step]
        total = total + shifted(acc.astype(jnp.bfloat16), "tz", 1).astype(jnp.float32)
    if left > 0:
        acc = own[left]
        for step in range(1, left):
            acc = shifted(acc.astype(jnp.bfloat16), "tz", -1).astype(jnp.float32) + own[left + step]
        total = total + shifted(acc.astype(jnp.bfloat16), "tz", -1).astype(jnp.float32)
    half = width // 2
    first = lax.axis_index("tx") == 0
    mine = jnp.where(first, total[:, :half], total[:, half:])
    other = jnp.where(first, total[:, half:], total[:, :half])
    arrived = shifted(other.astype(jnp.bfloat16), "tx", 1).astype(jnp.float32)
    return (mine + arrived).astype(jnp.bfloat16)


def passed_along(block, axis, distance):
    devices = range(lax.axis_size(axis))
    route = [(i - distance, i) for i in devices if i - distance in devices]
    return lax.ppermute(block, axis, route)


def silu_slope(value):
    sig = jax.nn.sigmoid(value)
    return sig * (1.0 + value * (1.0 - sig))


def conv_back(weights, padded, count):
    taps = weights.shape[0]
    return sum(
        (weights[k][None, :] * padded[taps - 1 - k : taps - 1 - k + count] for k in range(taps))
    )


def on_device(tokens, w_gate, w_conv_in, conv_weight, conv_bias, score_head, targets, loss_mask):
    rows = tokens.shape[0]
    chans = w_gate.shape[1]
    taps = conv_weight.shape[0]
    piece = gather_features(tokens)
    gate_acc = jnp.dot(piece, w_gate, preferred_element_type=jnp.float32)
    xin_acc = jnp.dot(piece, w_conv_in, preferred_element_type=jnp.float32)
    gate16 = lax.optimization_barrier(gate_acc.astype(jnp.bfloat16))
    zgate = gate16.astype(jnp.float32)
    xin16 = lax.optimization_barrier(xin_acc.astype(jnp.bfloat16))
    before = passed_along(xin16[rows - (taps - 1) :], "seq", 1)
    padded = jnp.concatenate([before, xin16], axis=0).astype(jnp.float32)
    conv_out = conv_bias[None, :] + sum(
        (conv_weight[k][None, :] * padded[k : k + rows] for k in range(taps))
    )
    active = jax.nn.silu(conv_out)
    sgate = jax.nn.silu(zgate)
    gated = (active * sgate).astype(jnp.bfloat16)
    scores = score_head.shape[0]
    onehot = (targets[:, None] == jnp.arange(scores, dtype=jnp.int32)[None, :]).astype(jnp.bfloat16)
    picked = jnp.dot(onehot, score_head, preferred_element_type=jnp.float32)
    dgated = loss_mask.astype(jnp.float32)[:, None] * picked
    dgate16 = (dgated * active * silu_slope(zgate)).astype(jnp.bfloat16)
    dconv = dgated * sgate * silu_slope(conv_out)
    edge_zeros = jnp.zeros((taps - 1, chans), jnp.float32)
    local = conv_back(conv_weight, jnp.concatenate([dconv, edge_zeros], axis=0), rows)
    front = conv_back(
        conv_weight, jnp.concatenate([edge_zeros, dconv[: taps - 1]], axis=0), taps - 1
    )
    arrived = passed_along(front, "seq", -1)
    dxin = jnp.concatenate(
        [local[: rows - (taps - 1)], local[rows - (taps - 1) :] + arrived], axis=0
    )
    dxin16 = dxin.astype(jnp.bfloat16)
    spec = (((1,), (1,)), ((), ()))
    terms = lax.dot_general(dgate16, w_gate, spec, preferred_element_type=jnp.float32)
    terms = terms + lax.dot_general(dxin16, w_conv_in, spec, preferred_element_type=jnp.float32)
    d_tokens = scatter_features(terms.astype(jnp.bfloat16))
    return (gated, d_tokens)


def solution(mesh):
    seq, tp = mesh.shape["seq"], mesh.shape["tp"]
    mesh = Mesh(mesh.devices.reshape(seq, tp // 2, 2), ("seq", "tz", "tx"))
    placed = (
        P("seq", TP),
        P(None, TP),
        P(None, TP),
        P(None, TP),
        P(TP),
        P(None, TP),
        P("seq"),
        P("seq"),
    )
    return jax.shard_map(
        on_device,
        mesh=mesh,
        in_specs=placed,
        out_specs=(P("seq", TP), P("seq", TP)),
        check_vma=False,
    )
```

```python
import jax
import jax.numpy as jnp
from jax import lax
from jax.sharding import Mesh
from jax.sharding import PartitionSpec as P

TP = ("tz", "tx")


def shifted(block, axis, distance):
    size = lax.axis_size(axis)
    return lax.ppermute(block, axis, [(i, (i + distance) % size) for i in range(size)])


def halves_in_order(mine, other):
    first = lax.axis_index("tx") == 0
    return jnp.where(first, jnp.concatenate([mine, other], 1), jnp.concatenate([other, mine], 1))


def gather_features(tokens):
    rows = tokens.shape[0]
    pair = halves_in_order(tokens, shifted(tokens, "tx", 1))
    count = lax.axis_size("tz")
    blocks = [pair] * count
    ahead = pair
    behind = pair
    for step in range(1, count // 2 + 1):
        ahead = shifted(ahead, "tz", 1)
        blocks[-step % count] = ahead
        if step < count - step:
            behind = shifted(behind, "tz", -1)
            blocks[step] = behind
    stacked = jnp.stack(blocks, 0)
    doubled = jnp.concatenate([stacked, stacked], 0)
    start = (count - lax.axis_index("tz")) % count
    ordered = lax.dynamic_slice_in_dim(doubled, start, count, 0)
    return ordered.transpose(1, 0, 2).reshape(rows, -1)


def scatter_features(terms16):
    rows = terms16.shape[0]
    count = lax.axis_size("tz")
    width = terms16.shape[1] // count
    per_dest = terms16.reshape(rows, count, width).transpose(1, 0, 2)
    doubled = jnp.concatenate([per_dest, per_dest], 0)
    own = lax.dynamic_slice_in_dim(doubled, lax.axis_index("tz"), count, 0).astype(jnp.float32)
    total = ring_reduce(own) if count != 16 else stride_two_reduce(own)
    half = width // 2
    first = lax.axis_index("tx") == 0
    mine = jnp.where(first, total[:, :half], total[:, half:])
    other = jnp.where(first, total[:, half:], total[:, :half])
    arrived = shifted(other.astype(jnp.bfloat16), "tx", 1).astype(jnp.float32)
    return (mine + arrived).astype(jnp.bfloat16)


def hop(acc, distance):
    return shifted(acc.astype(jnp.bfloat16), "tz", distance).astype(jnp.float32)


def ring_reduce(own):
    count = own.shape[0]
    right = count - 1 - count // 2
    left = count // 2
    total = own[0]
    if right > 0:
        acc = own[right]
        for step in range(1, right):
            acc = hop(acc, 1) + own[right - step]
        total = total + hop(acc, 1)
    if left > 0:
        acc = own[left]
        for step in range(1, left):
            acc = hop(acc, -1) + own[left + step]
        total = total + hop(acc, -1)
    return total


def stride_two_reduce(own):
    ahead = jnp.stack([own[7], own[8]])
    behind = jnp.stack([own[9], own[10]])
    total = own[0]
    for step in range(1, 4):
        ahead = hop(ahead, 2) + jnp.stack([own[7 - 2 * step], own[8 - 2 * step]])
        got = hop(behind, -2)
        if step < 3:
            behind = got + jnp.stack([own[9 + 2 * step], own[10 + 2 * step]])
        else:
            total = total + got[1]
            behind_odd = got[0] + own[15]
    return total + hop(ahead[0], 1) + hop(ahead[1], 2) + hop(behind_odd, -1)


def passed_along(block, axis, distance):
    devices = range(lax.axis_size(axis))
    route = [(i - distance, i) for i in devices if i - distance in devices]
    return lax.ppermute(block, axis, route)


def silu_slope(value):
    sig = jax.nn.sigmoid(value)
    return sig * (1.0 + value * (1.0 - sig))


def conv_back(weights, padded, count):
    taps = weights.shape[0]
    return sum(
        (weights[k][None, :] * padded[taps - 1 - k : taps - 1 - k + count] for k in range(taps))
    )


def on_device(tokens, w_gate, w_conv_in, conv_weight, conv_bias, score_head, targets, loss_mask):
    rows = tokens.shape[0]
    chans = w_gate.shape[1]
    taps = conv_weight.shape[0]
    piece = gather_features(tokens)
    gate_acc = jnp.dot(piece, w_gate, preferred_element_type=jnp.float32)
    xin_acc = jnp.dot(piece, w_conv_in, preferred_element_type=jnp.float32)
    gate16 = lax.optimization_barrier(gate_acc.astype(jnp.bfloat16))
    zgate = gate16.astype(jnp.float32)
    xin16 = lax.optimization_barrier(xin_acc.astype(jnp.bfloat16))
    before = passed_along(xin16[rows - (taps - 1) :], "seq", 1)
    padded = jnp.concatenate([before, xin16], axis=0).astype(jnp.float32)
    conv_out = conv_bias[None, :] + sum(
        (conv_weight[k][None, :] * padded[k : k + rows] for k in range(taps))
    )
    active = jax.nn.silu(conv_out)
    sgate = jax.nn.silu(zgate)
    gated = (active * sgate).astype(jnp.bfloat16)
    scores = score_head.shape[0]
    onehot = (targets[:, None] == jnp.arange(scores, dtype=jnp.int32)[None, :]).astype(jnp.bfloat16)
    picked = jnp.dot(onehot, score_head, preferred_element_type=jnp.float32)
    dgated = loss_mask.astype(jnp.float32)[:, None] * picked
    dgate16 = (dgated * active * silu_slope(zgate)).astype(jnp.bfloat16)
    dconv = dgated * sgate * silu_slope(conv_out)
    edge_zeros = jnp.zeros((taps - 1, chans), jnp.float32)
    local = conv_back(conv_weight, jnp.concatenate([dconv, edge_zeros], axis=0), rows)
    front = conv_back(
        conv_weight, jnp.concatenate([edge_zeros, dconv[: taps - 1]], axis=0), taps - 1
    )
    arrived = passed_along(front, "seq", -1)
    dxin = jnp.concatenate(
        [local[: rows - (taps - 1)], local[rows - (taps - 1) :] + arrived], axis=0
    )
    dxin16 = dxin.astype(jnp.bfloat16)
    spec = (((1,), (1,)), ((), ()))
    terms = lax.dot_general(dgate16, w_gate, spec, preferred_element_type=jnp.float32)
    terms = terms + lax.dot_general(dxin16, w_conv_in, spec, preferred_element_type=jnp.float32)
    d_tokens = scatter_features(terms.astype(jnp.bfloat16))
    return (gated, d_tokens)


def solution(mesh):
    seq, tp = mesh.shape["seq"], mesh.shape["tp"]
    mesh = Mesh(mesh.devices.reshape(seq, tp // 2, 2), ("seq", "tz", "tx"))
    placed = (
        P("seq", TP),
        P(None, TP),
        P(None, TP),
        P(None, TP),
        P(TP),
        P(None, TP),
        P("seq"),
        P("seq"),
    )
    return jax.shard_map(
        on_device,
        mesh=mesh,
        in_specs=placed,
        out_specs=(P("seq", TP), P("seq", TP)),
        check_vma=False,
    )
```

```python
import jax
import jax.numpy as jnp
from jax import lax
from jax.sharding import Mesh
from jax.sharding import PartitionSpec as P

TP = ("tz", "tx")


def shifted(block, axis, distance):
    size = lax.axis_size(axis)
    return lax.ppermute(block, axis, [(i, (i + distance) % size) for i in range(size)])


def halves_in_order(mine, other):
    first = lax.axis_index("tx") == 0
    return jnp.where(first, jnp.concatenate([mine, other], 1), jnp.concatenate([other, mine], 1))


def gathered_blocks(tokens):
    pair = halves_in_order(tokens, shifted(tokens, "tx", 1))
    count = lax.axis_size("tz")
    here = lax.axis_index("tz")
    found = [(pair, here)]
    ahead = pair
    behind = pair
    for step in range(1, count // 2 + 1):
        ahead = shifted(ahead, "tz", 1)
        found.append((ahead, (here - step) % count))
        if step < count - step:
            behind = shifted(behind, "tz", -1)
            found.append((behind, (here + step) % count))
    return found


def project(found, weights):
    width = found[0][0].shape[1]
    total = None
    for block, place in found:
        rows = lax.dynamic_slice_in_dim(weights, place * width, width, 0)
        part = jnp.dot(block, rows, preferred_element_type=jnp.float32)
        total = part if total is None else total + part
    return total


def scatter_features(make_block):
    count = lax.axis_size("tz")
    here = lax.axis_index("tz")
    own = lambda offset: make_block((here + offset) % count).astype(jnp.float32)
    right = count - 1 - count // 2
    left = count // 2
    total = None
    if right > 0:
        acc = own(right)
        for step in range(1, right):
            acc = hop(acc, 1) + own(right - step)
        total = hop(acc, 1)
    if left > 0:
        acc = own(left)
        for step in range(1, left):
            acc = hop(acc, -1) + own(left + step)
        total = hop(acc, -1) if total is None else total + hop(acc, -1)
    total = own(0) if total is None else total + own(0)
    half = total.shape[1] // 2
    first = lax.axis_index("tx") == 0
    mine = jnp.where(first, total[:, :half], total[:, half:])
    other = jnp.where(first, total[:, half:], total[:, :half])
    arrived = shifted(other.astype(jnp.bfloat16), "tx", 1).astype(jnp.float32)
    return (mine + arrived).astype(jnp.bfloat16)


def hop(acc, distance):
    return shifted(acc.astype(jnp.bfloat16), "tz", distance).astype(jnp.float32)


def passed_along(block, axis, distance):
    devices = range(lax.axis_size(axis))
    route = [(i - distance, i) for i in devices if i - distance in devices]
    return lax.ppermute(block, axis, route)


def silu_slope(value):
    sig = jax.nn.sigmoid(value)
    return sig * (1.0 + value * (1.0 - sig))


def conv_back(weights, padded, count):
    taps = weights.shape[0]
    return sum(
        (weights[k][None, :] * padded[taps - 1 - k : taps - 1 - k + count] for k in range(taps))
    )


def on_device(tokens, w_gate, w_conv_in, conv_weight, conv_bias, score_head, targets, loss_mask):
    rows = tokens.shape[0]
    chans = w_gate.shape[1]
    taps = conv_weight.shape[0]
    found = gathered_blocks(tokens)
    gate_acc = project(found, w_gate)
    xin_acc = project(found, w_conv_in)
    gate16 = lax.optimization_barrier(gate_acc.astype(jnp.bfloat16))
    zgate = gate16.astype(jnp.float32)
    xin16 = lax.optimization_barrier(xin_acc.astype(jnp.bfloat16))
    before = passed_along(xin16[rows - (taps - 1) :], "seq", 1)
    padded = jnp.concatenate([before, xin16], axis=0).astype(jnp.float32)
    conv_out = conv_bias[None, :] + sum(
        (conv_weight[k][None, :] * padded[k : k + rows] for k in range(taps))
    )
    active = jax.nn.silu(conv_out)
    sgate = jax.nn.silu(zgate)
    gated = (active * sgate).astype(jnp.bfloat16)
    scores = score_head.shape[0]
    onehot = (targets[:, None] == jnp.arange(scores, dtype=jnp.int32)[None, :]).astype(jnp.bfloat16)
    picked = jnp.dot(onehot, score_head, preferred_element_type=jnp.float32)
    dgated = loss_mask.astype(jnp.float32)[:, None] * picked
    dgate16 = (dgated * active * silu_slope(zgate)).astype(jnp.bfloat16)
    dconv = dgated * sgate * silu_slope(conv_out)
    edge_zeros = jnp.zeros((taps - 1, chans), jnp.float32)
    local = conv_back(conv_weight, jnp.concatenate([dconv, edge_zeros], axis=0), rows)
    front = conv_back(
        conv_weight, jnp.concatenate([edge_zeros, dconv[: taps - 1]], axis=0), taps - 1
    )
    arrived = passed_along(front, "seq", -1)
    dxin = jnp.concatenate(
        [local[: rows - (taps - 1)], local[rows - (taps - 1) :] + arrived], axis=0
    )
    dxin16 = dxin.astype(jnp.bfloat16)
    spec = (((1,), (1,)), ((), ()))
    width = 2 * tokens.shape[1]

    def block_terms(place):
        gate_rows = lax.dynamic_slice_in_dim(w_gate, place * width, width, 0)
        conv_rows = lax.dynamic_slice_in_dim(w_conv_in, place * width, width, 0)
        part = lax.dot_general(dgate16, gate_rows, spec, preferred_element_type=jnp.float32)
        part = part + lax.dot_general(dxin16, conv_rows, spec, preferred_element_type=jnp.float32)
        return part.astype(jnp.bfloat16)

    d_tokens = scatter_features(block_terms)
    return (gated, d_tokens)


def solution(mesh):
    seq, tp = mesh.shape["seq"], mesh.shape["tp"]
    mesh = Mesh(mesh.devices.reshape(seq, tp // 2, 2), ("seq", "tz", "tx"))
    placed = (
        P("seq", TP),
        P(None, TP),
        P(None, TP),
        P(None, TP),
        P(TP),
        P(None, TP),
        P("seq"),
        P("seq"),
    )
    return jax.shard_map(
        on_device,
        mesh=mesh,
        in_specs=placed,
        out_specs=(P("seq", TP), P("seq", TP)),
        check_vma=False,
    )
```

```python
import jax
import jax.numpy as jnp
from jax import lax
from jax.sharding import Mesh
from jax.sharding import PartitionSpec as P

TP = ("tz", "tx")


def shifted(block, axis, distance):
    size = lax.axis_size(axis)
    return lax.ppermute(block, axis, [(i, (i + distance) % size) for i in range(size)])


def halves_in_order(mine, other):
    first = lax.axis_index("tx") == 0
    return jnp.where(first, jnp.concatenate([mine, other], 1), jnp.concatenate([other, mine], 1))


def gathered_blocks(tokens):
    pair = halves_in_order(tokens, shifted(tokens, "tx", 1))
    count = lax.axis_size("tz")
    here = lax.axis_index("tz")
    found = [(pair, here)]
    ahead = pair
    behind = pair
    for step in range(1, count // 2 + 1):
        ahead = shifted(ahead, "tz", 1)
        found.append((ahead, (here - step) % count))
        if step < count - step:
            behind = shifted(behind, "tz", -1)
            found.append((behind, (here + step) % count))
    return found


def project(found, weights):
    width = found[0][0].shape[1]
    total = None
    for block, place in found:
        rows = lax.dynamic_slice_in_dim(weights, place * width, width, 0)
        part = jnp.dot(block, rows, preferred_element_type=jnp.float32)
        total = part if total is None else total + part
    return total


def scatter_features(make_block):
    count = lax.axis_size("tz")
    here = lax.axis_index("tz")
    own = lambda offset: make_block((here + offset) % count).astype(jnp.float32)
    right = count - 1 - count // 2
    left = count // 2
    total = None
    if right > 0:
        acc = own(right)
        for step in range(1, right):
            acc = hop(acc, 1) + own(right - step)
        total = hop(acc, 1)
    if left > 0:
        acc = own(left)
        for step in range(1, left):
            acc = hop(acc, -1) + own(left + step)
        total = hop(acc, -1) if total is None else total + hop(acc, -1)
    total = own(0) if total is None else total + own(0)
    half = total.shape[1] // 2
    first = lax.axis_index("tx") == 0
    mine = jnp.where(first, total[:, :half], total[:, half:])
    other = jnp.where(first, total[:, half:], total[:, :half])
    arrived = shifted(other.astype(jnp.bfloat16), "tx", 1).astype(jnp.float32)
    return (mine + arrived).astype(jnp.bfloat16)


def hop(acc, distance):
    return shifted(acc.astype(jnp.bfloat16), "tz", distance).astype(jnp.float32)


def passed_along(block, axis, distance):
    devices = range(lax.axis_size(axis))
    route = [(i - distance, i) for i in devices if i - distance in devices]
    return lax.ppermute(block, axis, route)


def silu_slope(value):
    sig = jax.nn.sigmoid(value)
    return sig * (1.0 + value * (1.0 - sig))


def conv_back(weights, padded, count):
    taps = weights.shape[0]
    return sum(
        (weights[k][None, :] * padded[taps - 1 - k : taps - 1 - k + count] for k in range(taps))
    )


def on_device(tokens, w_gate, w_conv_in, conv_weight, conv_bias, score_head, targets, loss_mask):
    rows = tokens.shape[0]
    chans = w_gate.shape[1]
    taps = conv_weight.shape[0]
    found = gathered_blocks(tokens)
    gate_acc = project(found, w_gate)
    xin_acc = project(found, w_conv_in)
    gate16 = lax.optimization_barrier(gate_acc.astype(jnp.bfloat16))
    zgate = gate16.astype(jnp.float32)
    xin16 = lax.optimization_barrier(xin_acc.astype(jnp.bfloat16))
    before = passed_along(xin16[rows - (taps - 1) :], "seq", 1)
    padded = jnp.concatenate([before, xin16], axis=0).astype(jnp.float32)
    conv_out = conv_bias[None, :] + sum(
        (conv_weight[k][None, :] * padded[k : k + rows] for k in range(taps))
    )
    active = jax.nn.silu(conv_out)
    sgate = jax.nn.silu(zgate)
    gated = (active * sgate).astype(jnp.bfloat16)
    scores = score_head.shape[0]
    onehot = (targets[:, None] == jnp.arange(scores, dtype=jnp.int32)[None, :]).astype(jnp.bfloat16)
    picked = jnp.dot(onehot, score_head, preferred_element_type=jnp.float32)
    dgated = loss_mask.astype(jnp.float32)[:, None] * picked
    dgate16 = (dgated * active * silu_slope(zgate)).astype(jnp.bfloat16)
    dconv = dgated * sgate * silu_slope(conv_out)
    edge_zeros = jnp.zeros((taps - 1, chans), jnp.float32)
    local = conv_back(conv_weight, jnp.concatenate([dconv, edge_zeros], axis=0), rows)
    front = conv_back(
        conv_weight, jnp.concatenate([edge_zeros, dconv[: taps - 1]], axis=0), taps - 1
    )
    arrived = passed_along(front, "seq", -1)
    cut = rows - (taps - 1)
    top16 = local[:cut].astype(jnp.bfloat16)
    tail16 = (local[cut:] + arrived).astype(jnp.bfloat16)
    spec = (((1,), (1,)), ((), ()))
    width = 2 * tokens.shape[1]

    def block_terms(place):
        gate_rows = lax.dynamic_slice_in_dim(w_gate, place * width, width, 0)
        conv_rows = lax.dynamic_slice_in_dim(w_conv_in, place * width, width, 0)
        parts = []
        for gate_part, conv_part in ((dgate16[:cut], top16), (dgate16[cut:], tail16)):
            part = lax.dot_general(gate_part, gate_rows, spec, preferred_element_type=jnp.float32)
            part = part + lax.dot_general(conv_part, conv_rows, spec, preferred_element_type=jnp.float32)
            parts.append(part.astype(jnp.bfloat16))
        return jnp.concatenate(parts, 0)

    d_tokens = scatter_features(block_terms)
    return (gated, d_tokens)


def solution(mesh):
    seq, tp = mesh.shape["seq"], mesh.shape["tp"]
    mesh = Mesh(mesh.devices.reshape(seq, tp // 2, 2), ("seq", "tz", "tx"))
    placed = (
        P("seq", TP),
        P(None, TP),
        P(None, TP),
        P(None, TP),
        P(TP),
        P(None, TP),
        P("seq"),
        P("seq"),
    )
    return jax.shard_map(
        on_device,
        mesh=mesh,
        in_specs=placed,
        out_specs=(P("seq", TP), P("seq", TP)),
        check_vma=False,
    )
```

```python
import jax
import jax.numpy as jnp
from jax import lax
from jax.sharding import Mesh
from jax.sharding import PartitionSpec as P

TP = ("tz", "tx")


def shifted(block, axis, distance):
    size = lax.axis_size(axis)
    return lax.ppermute(block, axis, [(i, (i + distance) % size) for i in range(size)])


def halves_in_order(mine, other):
    first = lax.axis_index("tx") == 0
    return jnp.where(first, jnp.concatenate([mine, other], 1), jnp.concatenate([other, mine], 1))


def gathered_blocks(tokens):
    pair = halves_in_order(tokens, shifted(tokens, "tx", 1))
    count = lax.axis_size("tz")
    here = lax.axis_index("tz")
    found = [(pair, here)]
    ahead = pair
    behind = pair
    for step in range(1, count // 2 + 1):
        ahead = shifted(ahead, "tz", 1)
        found.append((ahead, (here - step) % count))
        if step < count - step:
            behind = shifted(behind, "tz", -1)
            found.append((behind, (here + step) % count))
    return found


def project(found, weights):
    width = found[0][0].shape[1]
    total = None
    for block, place in found:
        rows = lax.dynamic_slice_in_dim(weights, place * width, width, 0)
        part = jnp.dot(block, rows, preferred_element_type=jnp.float32)
        total = part if total is None else total + part
    return total


def scatter_features(make_block):
    count = lax.axis_size("tz")
    here = lax.axis_index("tz")
    own = lambda offset: make_block((here + offset) % count).astype(jnp.float32)
    right = count - 1 - count // 2
    left = count // 2
    total = None
    if right > 0:
        acc = own(right)
        for step in range(1, right):
            acc = hop(acc, 1) + own(right - step)
        total = hop(acc, 1)
    if left > 0:
        acc = own(left)
        for step in range(1, left):
            acc = hop(acc, -1) + own(left + step)
        total = hop(acc, -1) if total is None else total + hop(acc, -1)
    total = own(0) if total is None else total + own(0)
    half = total.shape[1] // 2
    first = lax.axis_index("tx") == 0
    mine = jnp.where(first, total[:, :half], total[:, half:])
    other = jnp.where(first, total[:, half:], total[:, :half])
    arrived = shifted(other.astype(jnp.bfloat16), "tx", 1).astype(jnp.float32)
    return (mine + arrived).astype(jnp.bfloat16)


def hop(acc, distance):
    return shifted(acc.astype(jnp.bfloat16), "tz", distance).astype(jnp.float32)


def passed_along(block, axis, distance):
    devices = range(lax.axis_size(axis))
    route = [(i - distance, i) for i in devices if i - distance in devices]
    return lax.ppermute(block, axis, route)


def silu_slope(value):
    sig = jax.nn.sigmoid(value)
    return sig * (1.0 + value * (1.0 - sig))


def conv_back(weights, padded, count):
    taps = weights.shape[0]
    return sum(
        (weights[k][None, :] * padded[taps - 1 - k : taps - 1 - k + count] for k in range(taps))
    )


def on_device(tokens, w_gate, w_conv_in, conv_weight, conv_bias, score_head, targets, loss_mask):
    rows = tokens.shape[0]
    chans = w_gate.shape[1]
    taps = conv_weight.shape[0]
    found = gathered_blocks(tokens)
    both = jnp.concatenate([w_gate, w_conv_in], axis=1)
    both_acc = project(found, both)
    gate_acc = both_acc[:, :chans]
    xin_acc = both_acc[:, chans:]
    gate16 = lax.optimization_barrier(gate_acc.astype(jnp.bfloat16))
    zgate = gate16.astype(jnp.float32)
    xin16 = lax.optimization_barrier(xin_acc.astype(jnp.bfloat16))
    before = passed_along(xin16[rows - (taps - 1) :], "seq", 1)
    padded = jnp.concatenate([before, xin16], axis=0).astype(jnp.float32)
    conv_out = conv_bias[None, :] + sum(
        (conv_weight[k][None, :] * padded[k : k + rows] for k in range(taps))
    )
    active = jax.nn.silu(conv_out)
    sgate = jax.nn.silu(zgate)
    gated = (active * sgate).astype(jnp.bfloat16)
    scores = score_head.shape[0]
    onehot = (targets[:, None] == jnp.arange(scores, dtype=jnp.int32)[None, :]).astype(jnp.bfloat16)
    picked = jnp.dot(onehot, score_head, preferred_element_type=jnp.float32)
    dgated = loss_mask.astype(jnp.float32)[:, None] * picked
    dgate16 = (dgated * active * silu_slope(zgate)).astype(jnp.bfloat16)
    dconv = dgated * sgate * silu_slope(conv_out)
    edge_zeros = jnp.zeros((taps - 1, chans), jnp.float32)
    local = conv_back(conv_weight, jnp.concatenate([dconv, edge_zeros], axis=0), rows)
    front = conv_back(
        conv_weight, jnp.concatenate([edge_zeros, dconv[: taps - 1]], axis=0), taps - 1
    )
    arrived = passed_along(front, "seq", -1)
    dxin = jnp.concatenate(
        [local[: rows - (taps - 1)], local[rows - (taps - 1) :] + arrived], axis=0
    )
    dxin16 = dxin.astype(jnp.bfloat16)
    spec = (((1,), (1,)), ((), ()))
    width = 2 * tokens.shape[1]

    grads16 = jnp.concatenate([dgate16, dxin16], axis=1)

    def block_terms(place):
        rows_of_both = lax.dynamic_slice_in_dim(both, place * width, width, 0)
        part = lax.dot_general(grads16, rows_of_both, spec, preferred_element_type=jnp.float32)
        return part.astype(jnp.bfloat16)

    d_tokens = scatter_features(block_terms)
    return (gated, d_tokens)


def solution(mesh):
    seq, tp = mesh.shape["seq"], mesh.shape["tp"]
    mesh = Mesh(mesh.devices.reshape(seq, tp // 2, 2), ("seq", "tz", "tx"))
    placed = (
        P("seq", TP),
        P(None, TP),
        P(None, TP),
        P(None, TP),
        P(TP),
        P(None, TP),
        P("seq"),
        P("seq"),
    )
    return jax.shard_map(
        on_device,
        mesh=mesh,
        in_specs=placed,
        out_specs=(P("seq", TP), P("seq", TP)),
        check_vma=False,
    )
```

```python
import jax
import jax.numpy as jnp
from jax import lax
from jax.sharding import Mesh
from jax.sharding import PartitionSpec as P

TP = ("tz", "tx")


def shifted(block, axis, distance):
    size = lax.axis_size(axis)
    return lax.ppermute(block, axis, [(i, (i + distance) % size) for i in range(size)])


def halves_in_order(mine, other):
    first = lax.axis_index("tx") == 0
    return jnp.where(first, jnp.concatenate([mine, other], 1), jnp.concatenate([other, mine], 1))


def gather_features(tokens):
    rows = tokens.shape[0]
    pair = halves_in_order(tokens, shifted(tokens, "tx", 1))
    count = lax.axis_size("tz")
    blocks = [pair] * count
    ahead = pair
    behind = pair
    for step in range(1, count // 2 + 1):
        ahead = shifted(ahead, "tz", 1)
        blocks[-step % count] = ahead
        if step < count - step:
            behind = shifted(behind, "tz", -1)
            blocks[step] = behind
    stacked = jnp.stack(blocks, 0)
    doubled = jnp.concatenate([stacked, stacked], 0)
    start = (count - lax.axis_index("tz")) % count
    ordered = lax.dynamic_slice_in_dim(doubled, start, count, 0)
    return ordered.transpose(1, 0, 2).reshape(rows, -1)


def scatter_features(make_block):
    count = lax.axis_size("tz")
    here = lax.axis_index("tz")
    own = lambda offset: make_block((here + offset) % count).astype(jnp.float32)
    right = count - 1 - count // 2
    left = count // 2
    total = None
    if right > 0:
        acc = own(right)
        for step in range(1, right):
            acc = hop(acc, 1) + own(right - step)
        total = hop(acc, 1)
    if left > 0:
        acc = own(left)
        for step in range(1, left):
            acc = hop(acc, -1) + own(left + step)
        total = hop(acc, -1) if total is None else total + hop(acc, -1)
    total = own(0) if total is None else total + own(0)
    half = total.shape[1] // 2
    first = lax.axis_index("tx") == 0
    mine = jnp.where(first, total[:, :half], total[:, half:])
    other = jnp.where(first, total[:, half:], total[:, :half])
    arrived = shifted(other.astype(jnp.bfloat16), "tx", 1).astype(jnp.float32)
    return (mine + arrived).astype(jnp.bfloat16)


def hop(acc, distance):
    return shifted(acc.astype(jnp.bfloat16), "tz", distance).astype(jnp.float32)


def passed_along(block, axis, distance):
    devices = range(lax.axis_size(axis))
    route = [(i - distance, i) for i in devices if i - distance in devices]
    return lax.ppermute(block, axis, route)


def silu_slope(value):
    sig = jax.nn.sigmoid(value)
    return sig * (1.0 + value * (1.0 - sig))


def conv_back(weights, padded, count):
    taps = weights.shape[0]
    return sum(
        (weights[k][None, :] * padded[taps - 1 - k : taps - 1 - k + count] for k in range(taps))
    )


def on_device(tokens, w_gate, w_conv_in, conv_weight, conv_bias, score_head, targets, loss_mask):
    rows = tokens.shape[0]
    chans = w_gate.shape[1]
    taps = conv_weight.shape[0]
    piece = gather_features(tokens)
    gate_acc = jnp.dot(piece, w_gate, preferred_element_type=jnp.float32)
    xin_acc = jnp.dot(piece, w_conv_in, preferred_element_type=jnp.float32)
    gate16 = lax.optimization_barrier(gate_acc.astype(jnp.bfloat16))
    zgate = gate16.astype(jnp.float32)
    xin16 = lax.optimization_barrier(xin_acc.astype(jnp.bfloat16))
    before = passed_along(xin16[rows - (taps - 1) :], "seq", 1)
    padded = jnp.concatenate([before, xin16], axis=0).astype(jnp.float32)
    conv_out = conv_bias[None, :] + sum(
        (conv_weight[k][None, :] * padded[k : k + rows] for k in range(taps))
    )
    active = jax.nn.silu(conv_out)
    sgate = jax.nn.silu(zgate)
    gated = (active * sgate).astype(jnp.bfloat16)
    scores = score_head.shape[0]
    onehot = (targets[:, None] == jnp.arange(scores, dtype=jnp.int32)[None, :]).astype(jnp.bfloat16)
    picked = jnp.dot(onehot, score_head, preferred_element_type=jnp.float32)
    dgated = loss_mask.astype(jnp.float32)[:, None] * picked
    dgate16 = (dgated * active * silu_slope(zgate)).astype(jnp.bfloat16)
    dconv = dgated * sgate * silu_slope(conv_out)
    edge_zeros = jnp.zeros((taps - 1, chans), jnp.float32)
    local = conv_back(conv_weight, jnp.concatenate([dconv, edge_zeros], axis=0), rows)
    front = conv_back(
        conv_weight, jnp.concatenate([edge_zeros, dconv[: taps - 1]], axis=0), taps - 1
    )
    arrived = passed_along(front, "seq", -1)
    dxin = jnp.concatenate(
        [local[: rows - (taps - 1)], local[rows - (taps - 1) :] + arrived], axis=0
    )
    dxin16 = dxin.astype(jnp.bfloat16)
    spec = (((1,), (1,)), ((), ()))
    width = 2 * tokens.shape[1]

    def block_terms(place):
        gate_rows = lax.dynamic_slice_in_dim(w_gate, place * width, width, 0)
        conv_rows = lax.dynamic_slice_in_dim(w_conv_in, place * width, width, 0)
        part = lax.dot_general(dgate16, gate_rows, spec, preferred_element_type=jnp.float32)
        part = part + lax.dot_general(dxin16, conv_rows, spec, preferred_element_type=jnp.float32)
        return part.astype(jnp.bfloat16)

    d_tokens = scatter_features(block_terms)
    return (gated, d_tokens)


def solution(mesh):
    seq, tp = mesh.shape["seq"], mesh.shape["tp"]
    mesh = Mesh(mesh.devices.reshape(seq, tp // 2, 2), ("seq", "tz", "tx"))
    placed = (
        P("seq", TP),
        P(None, TP),
        P(None, TP),
        P(None, TP),
        P(TP),
        P(None, TP),
        P("seq"),
        P("seq"),
    )
    return jax.shard_map(
        on_device,
        mesh=mesh,
        in_specs=placed,
        out_specs=(P("seq", TP), P("seq", TP)),
        check_vma=False,
    )
```

```python
import jax
import jax.numpy as jnp
from jax import lax
from jax.sharding import Mesh
from jax.sharding import PartitionSpec as P

TP = ("tz", "tx")


def shifted(block, axis, distance):
    size = lax.axis_size(axis)
    return lax.ppermute(block, axis, [(i, (i + distance) % size) for i in range(size)])


def halves_in_order(mine, other):
    first = lax.axis_index("tx") == 0
    return jnp.where(first, jnp.concatenate([mine, other], 1), jnp.concatenate([other, mine], 1))


def across(block, dz):
    count = lax.axis_size("tz")
    route = [(z * 2 + x, (z + dz) % count * 2 + 1 - x) for z in range(count) for x in range(2)]
    return lax.ppermute(block, TP, route)


def gather_features(tokens):
    rows = tokens.shape[0]
    count = lax.axis_size("tz")
    pair = halves_in_order(tokens, shifted(tokens, "tx", 1))
    blocks = [pair] * count
    ahead = halves_in_order(shifted(tokens, "tz", 1), across(tokens, 1))
    blocks[-1 % count] = ahead
    behind = None
    if 1 < count - 1:
        behind = halves_in_order(shifted(tokens, "tz", -1), across(tokens, -1))
        blocks[1] = behind
    for step in range(2, count // 2 + 1):
        ahead = shifted(ahead, "tz", 1)
        blocks[-step % count] = ahead
        if step < count - step:
            behind = shifted(behind, "tz", -1)
            blocks[step] = behind
    stacked = jnp.stack(blocks, 0)
    doubled = jnp.concatenate([stacked, stacked], 0)
    start = (count - lax.axis_index("tz")) % count
    ordered = lax.dynamic_slice_in_dim(doubled, start, count, 0)
    return ordered.transpose(1, 0, 2).reshape(rows, -1)


def scatter_features(make_block):
    count = lax.axis_size("tz")
    here = lax.axis_index("tz")
    own = lambda offset: make_block((here + offset) % count).astype(jnp.float32)
    right = count - 1 - count // 2
    left = count // 2
    total = None
    if right > 0:
        acc = own(right)
        for step in range(1, right):
            acc = hop(acc, 1) + own(right - step)
        total = hop(acc, 1)
    if left > 0:
        acc = own(left)
        for step in range(1, left):
            acc = hop(acc, -1) + own(left + step)
        total = hop(acc, -1) if total is None else total + hop(acc, -1)
    total = own(0) if total is None else total + own(0)
    half = total.shape[1] // 2
    first = lax.axis_index("tx") == 0
    mine = jnp.where(first, total[:, :half], total[:, half:])
    other = jnp.where(first, total[:, half:], total[:, :half])
    arrived = shifted(other.astype(jnp.bfloat16), "tx", 1).astype(jnp.float32)
    return (mine + arrived).astype(jnp.bfloat16)


def hop(acc, distance):
    return shifted(acc.astype(jnp.bfloat16), "tz", distance).astype(jnp.float32)


def passed_along(block, axis, distance):
    devices = range(lax.axis_size(axis))
    route = [(i - distance, i) for i in devices if i - distance in devices]
    return lax.ppermute(block, axis, route)


def silu_slope(value):
    sig = jax.nn.sigmoid(value)
    return sig * (1.0 + value * (1.0 - sig))


def conv_back(weights, padded, count):
    taps = weights.shape[0]
    return sum(
        (weights[k][None, :] * padded[taps - 1 - k : taps - 1 - k + count] for k in range(taps))
    )


def on_device(tokens, w_gate, w_conv_in, conv_weight, conv_bias, score_head, targets, loss_mask):
    rows = tokens.shape[0]
    chans = w_gate.shape[1]
    taps = conv_weight.shape[0]
    piece = gather_features(tokens)
    gate_acc = jnp.dot(piece, w_gate, preferred_element_type=jnp.float32)
    xin_acc = jnp.dot(piece, w_conv_in, preferred_element_type=jnp.float32)
    gate16 = lax.optimization_barrier(gate_acc.astype(jnp.bfloat16))
    zgate = gate16.astype(jnp.float32)
    xin16 = lax.optimization_barrier(xin_acc.astype(jnp.bfloat16))
    before = passed_along(xin16[rows - (taps - 1) :], "seq", 1)
    padded = jnp.concatenate([before, xin16], axis=0).astype(jnp.float32)
    conv_out = conv_bias[None, :] + sum(
        (conv_weight[k][None, :] * padded[k : k + rows] for k in range(taps))
    )
    active = jax.nn.silu(conv_out)
    sgate = jax.nn.silu(zgate)
    gated = (active * sgate).astype(jnp.bfloat16)
    scores = score_head.shape[0]
    onehot = (targets[:, None] == jnp.arange(scores, dtype=jnp.int32)[None, :]).astype(jnp.bfloat16)
    picked = jnp.dot(onehot, score_head, preferred_element_type=jnp.float32)
    dgated = loss_mask.astype(jnp.float32)[:, None] * picked
    dgate16 = (dgated * active * silu_slope(zgate)).astype(jnp.bfloat16)
    dconv = dgated * sgate * silu_slope(conv_out)
    edge_zeros = jnp.zeros((taps - 1, chans), jnp.float32)
    local = conv_back(conv_weight, jnp.concatenate([dconv, edge_zeros], axis=0), rows)
    front = conv_back(
        conv_weight, jnp.concatenate([edge_zeros, dconv[: taps - 1]], axis=0), taps - 1
    )
    arrived = passed_along(front, "seq", -1)
    dxin = jnp.concatenate(
        [local[: rows - (taps - 1)], local[rows - (taps - 1) :] + arrived], axis=0
    )
    dxin16 = dxin.astype(jnp.bfloat16)
    spec = (((1,), (1,)), ((), ()))
    width = 2 * tokens.shape[1]

    def block_terms(place):
        gate_rows = lax.dynamic_slice_in_dim(w_gate, place * width, width, 0)
        conv_rows = lax.dynamic_slice_in_dim(w_conv_in, place * width, width, 0)
        part = lax.dot_general(dgate16, gate_rows, spec, preferred_element_type=jnp.float32)
        part = part + lax.dot_general(dxin16, conv_rows, spec, preferred_element_type=jnp.float32)
        return part.astype(jnp.bfloat16)

    d_tokens = scatter_features(block_terms)
    return (gated, d_tokens)


def solution(mesh):
    seq, tp = mesh.shape["seq"], mesh.shape["tp"]
    mesh = Mesh(mesh.devices.reshape(seq, tp // 2, 2), ("seq", "tz", "tx"))
    placed = (
        P("seq", TP),
        P(None, TP),
        P(None, TP),
        P(None, TP),
        P(TP),
        P(None, TP),
        P("seq"),
        P("seq"),
    )
    return jax.shard_map(
        on_device,
        mesh=mesh,
        in_specs=placed,
        out_specs=(P("seq", TP), P("seq", TP)),
        check_vma=False,
    )
```

```python
import jax
import jax.numpy as jnp
from jax import lax
from jax.sharding import Mesh
from jax.sharding import PartitionSpec as P

TP = ("tz", "tx")


def shifted(block, axis, distance):
    size = lax.axis_size(axis)
    return lax.ppermute(block, axis, [(i, (i + distance) % size) for i in range(size)])


def halves_in_order(mine, other):
    first = lax.axis_index("tx") == 0
    return jnp.where(first, jnp.concatenate([mine, other], 1), jnp.concatenate([other, mine], 1))


def gather_features(tokens):
    rows = tokens.shape[0]
    pair = halves_in_order(tokens, shifted(tokens, "tx", 1))
    count = lax.axis_size("tz")
    blocks = [pair] * count
    ahead = pair
    behind = pair
    for step in range(1, count // 2 + 1):
        ahead = shifted(ahead, "tz", 1)
        blocks[-step % count] = ahead
        if step < count - step:
            behind = shifted(behind, "tz", -1)
            blocks[step] = behind
    stacked = jnp.stack(blocks, 0)
    doubled = jnp.concatenate([stacked, stacked], 0)
    start = (count - lax.axis_index("tz")) % count
    ordered = lax.dynamic_slice_in_dim(doubled, start, count, 0)
    return ordered.transpose(1, 0, 2).reshape(rows, -1)


def scatter_features(make_block, operands):
    count = lax.axis_size("tz")
    here = lax.axis_index("tz")

    def own(offset, after=None):
        used = operands if after is None else lax.optimization_barrier((operands, after))[0]
        return make_block((here + offset) % count, *used).astype(jnp.float32)

    right = count - 1 - count // 2
    left = count // 2
    total = None
    last = None
    if right > 0:
        acc = own(right)
        coming = own(right - 1) if right > 1 else None
        for step in range(1, right):
            got = hop(acc, 1)
            acc = got + coming
            if step + 1 < right:
                coming = own(right - step - 1, got)
        total = hop(acc, 1)
        last = total
    if left > 0:
        acc = own(left)
        coming = own(left + 1) if left > 1 else None
        for step in range(1, left):
            got = hop(acc, -1)
            acc = got + coming
            if step + 1 < left:
                coming = own(left + step + 1, got)
        arrived_left = hop(acc, -1)
        total = arrived_left if total is None else total + arrived_left
        last = acc
    total = own(0, last) + (0.0 if total is None else total)
    half = total.shape[1] // 2
    first = lax.axis_index("tx") == 0
    mine = jnp.where(first, total[:, :half], total[:, half:])
    other = jnp.where(first, total[:, half:], total[:, :half])
    arrived = shifted(other.astype(jnp.bfloat16), "tx", 1).astype(jnp.float32)
    return (mine + arrived).astype(jnp.bfloat16)


def hop(acc, distance):
    return shifted(acc.astype(jnp.bfloat16), "tz", distance).astype(jnp.float32)


def passed_along(block, axis, distance):
    devices = range(lax.axis_size(axis))
    route = [(i - distance, i) for i in devices if i - distance in devices]
    return lax.ppermute(block, axis, route)


def silu_slope(value):
    sig = jax.nn.sigmoid(value)
    return sig * (1.0 + value * (1.0 - sig))


def conv_back(weights, padded, count):
    taps = weights.shape[0]
    return sum(
        (weights[k][None, :] * padded[taps - 1 - k : taps - 1 - k + count] for k in range(taps))
    )


def on_device(tokens, w_gate, w_conv_in, conv_weight, conv_bias, score_head, targets, loss_mask):
    rows = tokens.shape[0]
    chans = w_gate.shape[1]
    taps = conv_weight.shape[0]
    piece = gather_features(tokens)
    gate_acc = jnp.dot(piece, w_gate, preferred_element_type=jnp.float32)
    xin_acc = jnp.dot(piece, w_conv_in, preferred_element_type=jnp.float32)
    gate16 = lax.optimization_barrier(gate_acc.astype(jnp.bfloat16))
    zgate = gate16.astype(jnp.float32)
    xin16 = lax.optimization_barrier(xin_acc.astype(jnp.bfloat16))
    before = passed_along(xin16[rows - (taps - 1) :], "seq", 1)
    padded = jnp.concatenate([before, xin16], axis=0).astype(jnp.float32)
    conv_out = conv_bias[None, :] + sum(
        (conv_weight[k][None, :] * padded[k : k + rows] for k in range(taps))
    )
    active = jax.nn.silu(conv_out)
    sgate = jax.nn.silu(zgate)
    gated = (active * sgate).astype(jnp.bfloat16)
    scores = score_head.shape[0]
    onehot = (targets[:, None] == jnp.arange(scores, dtype=jnp.int32)[None, :]).astype(jnp.bfloat16)
    picked = jnp.dot(onehot, score_head, preferred_element_type=jnp.float32)
    dgated = loss_mask.astype(jnp.float32)[:, None] * picked
    dgate16 = (dgated * active * silu_slope(zgate)).astype(jnp.bfloat16)
    dconv = dgated * sgate * silu_slope(conv_out)
    edge_zeros = jnp.zeros((taps - 1, chans), jnp.float32)
    local = conv_back(conv_weight, jnp.concatenate([dconv, edge_zeros], axis=0), rows)
    front = conv_back(
        conv_weight, jnp.concatenate([edge_zeros, dconv[: taps - 1]], axis=0), taps - 1
    )
    arrived = passed_along(front, "seq", -1)
    dxin = jnp.concatenate(
        [local[: rows - (taps - 1)], local[rows - (taps - 1) :] + arrived], axis=0
    )
    dxin16 = dxin.astype(jnp.bfloat16)
    spec = (((1,), (1,)), ((), ()))
    width = 2 * tokens.shape[1]

    def block_terms(place, dgate16, dxin16):
        gate_rows = lax.dynamic_slice_in_dim(w_gate, place * width, width, 0)
        conv_rows = lax.dynamic_slice_in_dim(w_conv_in, place * width, width, 0)
        part = lax.dot_general(dgate16, gate_rows, spec, preferred_element_type=jnp.float32)
        part = part + lax.dot_general(dxin16, conv_rows, spec, preferred_element_type=jnp.float32)
        return part.astype(jnp.bfloat16)

    d_tokens = scatter_features(block_terms, (dgate16, dxin16))
    return (gated, d_tokens)


def solution(mesh):
    seq, tp = mesh.shape["seq"], mesh.shape["tp"]
    mesh = Mesh(mesh.devices.reshape(seq, tp // 2, 2), ("seq", "tz", "tx"))
    placed = (
        P("seq", TP),
        P(None, TP),
        P(None, TP),
        P(None, TP),
        P(TP),
        P(None, TP),
        P("seq"),
        P("seq"),
    )
    return jax.shard_map(
        on_device,
        mesh=mesh,
        in_specs=placed,
        out_specs=(P("seq", TP), P("seq", TP)),
        check_vma=False,
    )
```

```python
import jax
import jax.numpy as jnp
from jax import lax
from jax.sharding import Mesh
from jax.sharding import PartitionSpec as P

TP = ("tz", "tx")


def shifted(block, axis, distance):
    size = lax.axis_size(axis)
    return lax.ppermute(block, axis, [(i, (i + distance) % size) for i in range(size)])


def halves_in_order(mine, other):
    first = lax.axis_index("tx") == 0
    return jnp.where(first, jnp.concatenate([mine, other], 1), jnp.concatenate([other, mine], 1))


def gather_features(tokens):
    rows = tokens.shape[0]
    pair = halves_in_order(tokens, shifted(tokens, "tx", 1))
    count = lax.axis_size("tz")
    blocks = [pair] * count
    ahead = pair
    behind = pair
    for step in range(1, count // 2 + 1):
        ahead = shifted(ahead, "tz", 1)
        blocks[-step % count] = ahead
        if step < count - step:
            behind = shifted(behind, "tz", -1)
            blocks[step] = behind
    stacked = jnp.stack(blocks, 0)
    doubled = jnp.concatenate([stacked, stacked], 0)
    start = (count - lax.axis_index("tz")) % count
    ordered = lax.dynamic_slice_in_dim(doubled, start, count, 0)
    return ordered.transpose(1, 0, 2).reshape(rows, -1)


def across(block, dz):
    count = lax.axis_size("tz")
    route = [(z * 2 + x, (z + dz) % count * 2 + 1 - x) for z in range(count) for x in range(2)]
    return lax.ppermute(block, TP, route)


def scatter_features(make_block, operands):
    count = lax.axis_size("tz")
    here = lax.axis_index("tz")

    def own(offset, after=None):
        used = operands if after is None else lax.optimization_barrier((operands, after))[0]
        return make_block((here + offset) % count, *used).astype(jnp.float32)

    first = lax.axis_index("tx") == 0

    def split(block):
        half = block.shape[1] // 2
        mine = jnp.where(first, block[:, :half], block[:, half:])
        other = jnp.where(first, block[:, half:], block[:, :half])
        return mine, other

    right = count - 1 - count // 2
    left = count // 2
    partial = None
    if right > 0:
        acc = own(right)
        coming = own(right - 1) if right > 1 else None
        for step in range(1, right):
            got = hop(acc, 1)
            acc = got + coming
            if step + 1 < right:
                coming = own(right - step - 1, got)
        partial = hop(acc, 1)
    partial = own(0, partial) if partial is None else own(0, partial) + partial
    mine, other = split(partial)
    mine = mine + shifted(other.astype(jnp.bfloat16), "tx", 1).astype(jnp.float32)
    if left > 0:
        acc = own(left)
        coming = own(left + 1) if left > 1 else None
        for step in range(1, left):
            got = hop(acc, -1)
            acc = got + coming
            if step + 1 < left:
                coming = own(left + step + 1, got)
        ahead_mine, ahead_other = split(acc.astype(jnp.bfloat16))
        mine = mine + shifted(ahead_mine, "tz", -1).astype(jnp.float32)
        mine = mine + across(ahead_other, -1).astype(jnp.float32)
    return mine.astype(jnp.bfloat16)


def hop(acc, distance):
    return shifted(acc.astype(jnp.bfloat16), "tz", distance).astype(jnp.float32)


def passed_along(block, axis, distance):
    devices = range(lax.axis_size(axis))
    route = [(i - distance, i) for i in devices if i - distance in devices]
    return lax.ppermute(block, axis, route)


def silu_slope(value):
    sig = jax.nn.sigmoid(value)
    return sig * (1.0 + value * (1.0 - sig))


def conv_back(weights, padded, count):
    taps = weights.shape[0]
    return sum(
        (weights[k][None, :] * padded[taps - 1 - k : taps - 1 - k + count] for k in range(taps))
    )


def on_device(tokens, w_gate, w_conv_in, conv_weight, conv_bias, score_head, targets, loss_mask):
    rows = tokens.shape[0]
    chans = w_gate.shape[1]
    taps = conv_weight.shape[0]
    piece = gather_features(tokens)
    gate_acc = jnp.dot(piece, w_gate, preferred_element_type=jnp.float32)
    xin_acc = jnp.dot(piece, w_conv_in, preferred_element_type=jnp.float32)
    gate16 = lax.optimization_barrier(gate_acc.astype(jnp.bfloat16))
    zgate = gate16.astype(jnp.float32)
    xin16 = lax.optimization_barrier(xin_acc.astype(jnp.bfloat16))
    before = passed_along(xin16[rows - (taps - 1) :], "seq", 1)
    padded = jnp.concatenate([before, xin16], axis=0).astype(jnp.float32)
    conv_out = conv_bias[None, :] + sum(
        (conv_weight[k][None, :] * padded[k : k + rows] for k in range(taps))
    )
    active = jax.nn.silu(conv_out)
    sgate = jax.nn.silu(zgate)
    gated = (active * sgate).astype(jnp.bfloat16)
    scores = score_head.shape[0]
    onehot = (targets[:, None] == jnp.arange(scores, dtype=jnp.int32)[None, :]).astype(jnp.bfloat16)
    picked = jnp.dot(onehot, score_head, preferred_element_type=jnp.float32)
    dgated = loss_mask.astype(jnp.float32)[:, None] * picked
    dgate16 = (dgated * active * silu_slope(zgate)).astype(jnp.bfloat16)
    dconv = dgated * sgate * silu_slope(conv_out)
    edge_zeros = jnp.zeros((taps - 1, chans), jnp.float32)
    local = conv_back(conv_weight, jnp.concatenate([dconv, edge_zeros], axis=0), rows)
    front = conv_back(
        conv_weight, jnp.concatenate([edge_zeros, dconv[: taps - 1]], axis=0), taps - 1
    )
    arrived = passed_along(front, "seq", -1)
    dxin = jnp.concatenate(
        [local[: rows - (taps - 1)], local[rows - (taps - 1) :] + arrived], axis=0
    )
    dxin16 = dxin.astype(jnp.bfloat16)
    spec = (((1,), (1,)), ((), ()))
    width = 2 * tokens.shape[1]

    def block_terms(place, dgate16, dxin16):
        gate_rows = lax.dynamic_slice_in_dim(w_gate, place * width, width, 0)
        conv_rows = lax.dynamic_slice_in_dim(w_conv_in, place * width, width, 0)
        part = lax.dot_general(dgate16, gate_rows, spec, preferred_element_type=jnp.float32)
        part = part + lax.dot_general(dxin16, conv_rows, spec, preferred_element_type=jnp.float32)
        return part.astype(jnp.bfloat16)

    d_tokens = scatter_features(block_terms, (dgate16, dxin16))
    return (gated, d_tokens)


def solution(mesh):
    seq, tp = mesh.shape["seq"], mesh.shape["tp"]
    mesh = Mesh(mesh.devices.reshape(seq, tp // 2, 2), ("seq", "tz", "tx"))
    placed = (
        P("seq", TP),
        P(None, TP),
        P(None, TP),
        P(None, TP),
        P(TP),
        P(None, TP),
        P("seq"),
        P("seq"),
    )
    return jax.shard_map(
        on_device,
        mesh=mesh,
        in_specs=placed,
        out_specs=(P("seq", TP), P("seq", TP)),
        check_vma=False,
    )
```

```python
import jax
import jax.numpy as jnp
from jax import lax
from jax.sharding import Mesh
from jax.sharding import PartitionSpec as P

TP = ("tz", "tx")


def shifted(block, axis, distance):
    size = lax.axis_size(axis)
    return lax.ppermute(block, axis, [(i, (i + distance) % size) for i in range(size)])


def halves_in_order(mine, other):
    first = lax.axis_index("tx") == 0
    return jnp.where(first, jnp.concatenate([mine, other], 1), jnp.concatenate([other, mine], 1))


def gather_features(tokens):
    rows = tokens.shape[0]
    pair = halves_in_order(tokens, shifted(tokens, "tx", 1))
    count = lax.axis_size("tz")
    blocks = [pair] * count
    ahead = pair
    behind = pair
    for step in range(1, count // 2 + 1):
        ahead = shifted(ahead, "tz", 1)
        blocks[-step % count] = ahead
        if step < count - step:
            behind = shifted(behind, "tz", -1)
            blocks[step] = behind
    stacked = jnp.stack(blocks, 0)
    doubled = jnp.concatenate([stacked, stacked], 0)
    start = (count - lax.axis_index("tz")) % count
    ordered = lax.dynamic_slice_in_dim(doubled, start, count, 0)
    return ordered.transpose(1, 0, 2).reshape(rows, -1)


def scatter_features(make_block, operands):
    count = lax.axis_size("tz")
    here = lax.axis_index("tz")

    def own(offset, after=None):
        used = operands if after is None else lax.optimization_barrier((operands, after))[0]
        return make_block((here + offset) % count, *used).astype(jnp.float32)

    right = count - 1 - count // 2
    left = count // 2
    total = None
    last = None
    if right > 0:
        acc = own(right)
        coming = own(right - 1) if right > 1 else None
        for step in range(1, right):
            got = hop(acc, 1)
            acc = got + coming
            if step + 1 < right:
                coming = own(right - step - 1, got)
        total = hop(acc, 1)
        last = total
    if left > 0:
        acc = own(left)
        coming = own(left + 1) if left > 1 else None
        for step in range(1, left):
            got = hop(acc, -1)
            acc = got + coming
            if step + 1 < left:
                coming = own(left + step + 1, got)
        arrived_left = hop(acc, -1)
        total = arrived_left if total is None else total + arrived_left
        last = acc
    total = own(0, last) + (0.0 if total is None else total)
    half = total.shape[1] // 2
    first = lax.axis_index("tx") == 0
    mine = jnp.where(first, total[:, :half], total[:, half:])
    other = jnp.where(first, total[:, half:], total[:, :half])
    arrived = shifted(other.astype(jnp.bfloat16), "tx", 1).astype(jnp.float32)
    return (mine + arrived).astype(jnp.bfloat16)


def hop(acc, distance):
    return shifted(acc.astype(jnp.bfloat16), "tz", distance).astype(jnp.float32)


def passed_along(block, axis, distance):
    devices = range(lax.axis_size(axis))
    route = [(i - distance, i) for i in devices if i - distance in devices]
    return lax.ppermute(block, axis, route)


def silu_slope(value):
    sig = jax.nn.sigmoid(value)
    return sig * (1.0 + value * (1.0 - sig))


def conv_back(weights, padded, count):
    taps = weights.shape[0]
    return sum(
        (weights[k][None, :] * padded[taps - 1 - k : taps - 1 - k + count] for k in range(taps))
    )


def on_device(tokens, w_gate, w_conv_in, conv_weight, conv_bias, score_head, targets, loss_mask):
    rows = tokens.shape[0]
    chans = w_gate.shape[1]
    taps = conv_weight.shape[0]
    piece = gather_features(tokens)
    gate_acc = jnp.dot(piece, w_gate, preferred_element_type=jnp.float32)
    xin_acc = jnp.dot(piece, w_conv_in, preferred_element_type=jnp.float32)
    gate16 = lax.optimization_barrier(gate_acc.astype(jnp.bfloat16))
    zgate = gate16.astype(jnp.float32)
    xin16 = lax.optimization_barrier(xin_acc.astype(jnp.bfloat16))
    before = passed_along(xin16[rows - (taps - 1) :], "seq", 1)
    padded = jnp.concatenate([before, xin16], axis=0).astype(jnp.float32)
    conv_out = conv_bias[None, :] + sum(
        (conv_weight[k][None, :] * padded[k : k + rows] for k in range(taps))
    )
    active = jax.nn.silu(conv_out)
    sgate = jax.nn.silu(zgate)
    gated = (active * sgate).astype(jnp.bfloat16)
    scores = score_head.shape[0]
    onehot = (targets[:, None] == jnp.arange(scores, dtype=jnp.int32)[None, :]).astype(jnp.bfloat16)
    picked = jnp.dot(onehot, score_head, preferred_element_type=jnp.float32)
    dgated = loss_mask.astype(jnp.float32)[:, None] * picked
    dgate16 = (dgated * active * silu_slope(zgate)).astype(jnp.bfloat16)
    dconv = dgated * sgate * silu_slope(conv_out)
    edge_zeros = jnp.zeros((taps - 1, chans), jnp.float32)
    local = conv_back(conv_weight, jnp.concatenate([dconv, edge_zeros], axis=0), rows)
    front = conv_back(
        conv_weight, jnp.concatenate([edge_zeros, dconv[: taps - 1]], axis=0), taps - 1
    )
    arrived = passed_along(front, "seq", -1)
    dxin = jnp.concatenate(
        [local[: rows - (taps - 1)], local[rows - (taps - 1) :] + arrived], axis=0
    )
    dxin16 = dxin.astype(jnp.bfloat16)
    spec = (((1,), (1,)), ((), ()))
    width = 2 * tokens.shape[1]

    def block_terms(place, dgate16, dxin16):
        gate_rows = lax.dynamic_slice_in_dim(w_gate, place * width, width, 0)
        conv_rows = lax.dynamic_slice_in_dim(w_conv_in, place * width, width, 0)
        part = lax.optimization_barrier(lax.dot_general(dgate16, gate_rows, spec, preferred_element_type=jnp.float32))
        part = part + lax.dot_general(dxin16, conv_rows, spec, preferred_element_type=jnp.float32)
        return part.astype(jnp.bfloat16)

    d_tokens = scatter_features(block_terms, (dgate16, dxin16))
    return (gated, d_tokens)


def solution(mesh):
    seq, tp = mesh.shape["seq"], mesh.shape["tp"]
    mesh = Mesh(mesh.devices.reshape(seq, tp // 2, 2), ("seq", "tz", "tx"))
    placed = (
        P("seq", TP),
        P(None, TP),
        P(None, TP),
        P(None, TP),
        P(TP),
        P(None, TP),
        P("seq"),
        P("seq"),
    )
    return jax.shard_map(
        on_device,
        mesh=mesh,
        in_specs=placed,
        out_specs=(P("seq", TP), P("seq", TP)),
        check_vma=False,
    )
```

```python
import jax
import jax.numpy as jnp
from jax import lax
from jax.sharding import Mesh
from jax.sharding import PartitionSpec as P

TP = ("tz", "tx")


def shifted(block, axis, distance):
    size = lax.axis_size(axis)
    return lax.ppermute(block, axis, [(i, (i + distance) % size) for i in range(size)])


def halves_in_order(mine, other):
    first = lax.axis_index("tx") == 0
    return jnp.where(first, jnp.concatenate([mine, other], 1), jnp.concatenate([other, mine], 1))


def gather_features(tokens):
    rows = tokens.shape[0]
    pair = halves_in_order(tokens, shifted(tokens, "tx", 1))
    count = lax.axis_size("tz")
    blocks = [pair] * count
    ahead = pair
    behind = pair
    for step in range(1, count // 2 + 1):
        ahead = shifted(ahead, "tz", 1)
        blocks[-step % count] = ahead
        if step < count - step:
            behind = shifted(behind, "tz", -1)
            blocks[step] = behind
    stacked = jnp.stack(blocks, 0)
    doubled = jnp.concatenate([stacked, stacked], 0)
    start = (count - lax.axis_index("tz")) % count
    ordered = lax.dynamic_slice_in_dim(doubled, start, count, 0)
    return ordered.transpose(1, 0, 2).reshape(rows, -1)


def scatter_features(make_block, operands):
    count = lax.axis_size("tz")
    here = lax.axis_index("tz")

    def own(offset, after=None):
        used = operands if after is None else lax.optimization_barrier((operands, after))[0]
        return make_block((here + offset) % count, *used).astype(jnp.float32)

    right = count - 1 - count // 2
    left = count // 2
    total = None
    last = None
    if right > 0:
        acc = own(right)
        coming = own(right - 1) if right > 1 else None
        for step in range(1, right):
            got = hop(acc, 1)
            acc = got + coming
            if step + 1 < right:
                coming = own(right - step - 1, got)
        total = hop(acc, 1)
        last = total
    if left > 0:
        acc = own(left)
        coming = own(left + 1) if left > 1 else None
        for step in range(1, left):
            got = hop(acc, -1)
            acc = got + coming
            if step + 1 < left:
                coming = own(left + step + 1, got)
        arrived_left = hop(acc, -1)
        total = arrived_left if total is None else total + arrived_left
        last = acc
    total = own(0, last) + (0.0 if total is None else total)
    half = total.shape[1] // 2
    first = lax.axis_index("tx") == 0
    mine = jnp.where(first, total[:, :half], total[:, half:])
    other = jnp.where(first, total[:, half:], total[:, :half])
    arrived = shifted(other.astype(jnp.bfloat16), "tx", 1).astype(jnp.float32)
    return (mine + arrived).astype(jnp.bfloat16)


def hop(acc, distance):
    return shifted(acc.astype(jnp.bfloat16), "tz", distance).astype(jnp.float32)


def passed_along(block, axis, distance):
    devices = range(lax.axis_size(axis))
    route = [(i - distance, i) for i in devices if i - distance in devices]
    return lax.ppermute(block, axis, route)


def silu_slope(value):
    sig = jax.nn.sigmoid(value)
    return sig * (1.0 + value * (1.0 - sig))


def conv_back(weights, padded, count):
    taps = weights.shape[0]
    return sum(
        (weights[k][None, :] * padded[taps - 1 - k : taps - 1 - k + count] for k in range(taps))
    )


def on_device(tokens, w_gate, w_conv_in, conv_weight, conv_bias, score_head, targets, loss_mask):
    rows = tokens.shape[0]
    chans = w_gate.shape[1]
    taps = conv_weight.shape[0]
    piece = gather_features(tokens)
    gate_acc = jnp.dot(piece, w_gate, preferred_element_type=jnp.float32)
    xin_acc = jnp.dot(piece, w_conv_in, preferred_element_type=jnp.float32)
    gate16 = lax.optimization_barrier(gate_acc.astype(jnp.bfloat16))
    zgate = gate16.astype(jnp.float32)
    xin16 = lax.optimization_barrier(xin_acc.astype(jnp.bfloat16))
    tail = jnp.dot(piece[rows - (taps - 1) :], w_conv_in, preferred_element_type=jnp.float32)
    before = passed_along(tail.astype(jnp.bfloat16), "seq", 1)
    padded = jnp.concatenate([before, xin16], axis=0).astype(jnp.float32)
    conv_out = conv_bias[None, :] + sum(
        (conv_weight[k][None, :] * padded[k : k + rows] for k in range(taps))
    )
    active = jax.nn.silu(conv_out)
    sgate = jax.nn.silu(zgate)
    gated = (active * sgate).astype(jnp.bfloat16)
    scores = score_head.shape[0]
    onehot = (targets[:, None] == jnp.arange(scores, dtype=jnp.int32)[None, :]).astype(jnp.bfloat16)
    picked = jnp.dot(onehot, score_head, preferred_element_type=jnp.float32)
    dgated = loss_mask.astype(jnp.float32)[:, None] * picked
    dgate16 = (dgated * active * silu_slope(zgate)).astype(jnp.bfloat16)
    dconv = dgated * sgate * silu_slope(conv_out)
    edge_zeros = jnp.zeros((taps - 1, chans), jnp.float32)
    local = conv_back(conv_weight, jnp.concatenate([dconv, edge_zeros], axis=0), rows)
    front = conv_back(
        conv_weight, jnp.concatenate([edge_zeros, dconv[: taps - 1]], axis=0), taps - 1
    )
    arrived = passed_along(front, "seq", -1)
    dxin = jnp.concatenate(
        [local[: rows - (taps - 1)], local[rows - (taps - 1) :] + arrived], axis=0
    )
    dxin16 = dxin.astype(jnp.bfloat16)
    spec = (((1,), (1,)), ((), ()))
    width = 2 * tokens.shape[1]

    def block_terms(place, dgate16, dxin16):
        gate_rows = lax.dynamic_slice_in_dim(w_gate, place * width, width, 0)
        conv_rows = lax.dynamic_slice_in_dim(w_conv_in, place * width, width, 0)
        part = lax.dot_general(dgate16, gate_rows, spec, preferred_element_type=jnp.float32)
        part = part + lax.dot_general(dxin16, conv_rows, spec, preferred_element_type=jnp.float32)
        return part.astype(jnp.bfloat16)

    d_tokens = scatter_features(block_terms, (dgate16, dxin16))
    return (gated, d_tokens)


def solution(mesh):
    seq, tp = mesh.shape["seq"], mesh.shape["tp"]
    mesh = Mesh(mesh.devices.reshape(seq, tp // 2, 2), ("seq", "tz", "tx"))
    placed = (
        P("seq", TP),
        P(None, TP),
        P(None, TP),
        P(None, TP),
        P(TP),
        P(None, TP),
        P("seq"),
        P("seq"),
    )
    return jax.shard_map(
        on_device,
        mesh=mesh,
        in_specs=placed,
        out_specs=(P("seq", TP), P("seq", TP)),
        check_vma=False,
    )
```
